32 devices in a mesh: blk: 8 (over z, core), vb: 4 (over y, x).
Axes of the slice: x: 2, y: 2, z: 4, core: 2. Of those that a mesh axis runs over, the one named last changes fastest.
Arguments:
- amplitudes: float32 [32, 1024, 1024], P('blk', 'vb'), may hold values from -6 to 6
- integrals: float32 [2048, 1024], P('blk'), may hold values from -0.5 to 0.5
- row_orbitals: int32 [2048], P('blk'), may hold values from 0 to 1023
- pair_orbitals: int32 [32, 2], P('blk'), may hold values from 0 to 255
- occupied_energy: float32 [256], replicated, may hold values from -2 to -0.5
- virtual_energy: float32 [1024], replicated, may hold values from 0.5 to 3
Outputs:
- density: float32 [32, 1024, 1024], P('blk', 'vb')
The draws below stay inside these ranges and needn't reach their ends.
All inputs are finite; a program needn't handle non-finite values.
Results may differ from the reference program's by a relative error of at most 0.0003.
Values sent between devices are 32-bit elements; how exact they have to be, the bound alone decides.
No kernel may reach another device: no remote copies, remote signals or barrier semaphores. Data moves between devices by JAX's collectives and lax.ppermute only.
A program may use at most 64 MiB of HBM per device.

```python
import jax
import jax.numpy as jnp
from jax import lax

V = 1024
NOCC = 256
CH = 256
PAIR_DEV = 4
HOPS = 5
PAIRS = 32
ROWS = 2048
N_BLK = 8


def with_ends(entries, key, least, top_value):
    place = [jax.random.randint(jax.random.fold_in(key, axis), (), 0, length) for axis, length in enumerate(entries.shape)]
    longest = entries.shape.index(max(entries.shape))
    neighbour = place[:longest] + [(place[longest] + 1) % entries.shape[longest]] + place[longest + 1:]
    return entries.at[tuple(place)].set(least).at[tuple(neighbour)].set(top_value)


def block_levels(key, extent, split, least, high):
    gain = 1.0
    for dim, blocks in split:
        heights = jax.random.uniform(jax.random.fold_in(jax.random.fold_in(key, 6), dim), (blocks,), jnp.float32, least / len(split), high / len(split))
        gain = gain * jnp.repeat(jnp.exp(heights), extent[dim] // blocks).reshape((-1,) + (1,) * (len(extent) - 1 - dim))
    return gain


def normal_values(own_key, dims, scale, limit, split=(), kind=jnp.bfloat16):
    factor_of = block_levels(own_key, dims, split, -0.22, 0.18) if split else 1.0
    drawn = jax.random.normal(own_key, dims, jnp.float32) * scale * factor_of
    return jnp.minimum(jnp.maximum(drawn, -limit), limit).astype(kind)


def setup_inputs(seed: int = 0) -> dict:
    keys = jax.random.split(jax.random.key(seed), 7)
    return {
        "amplitudes": normal_values(keys[0], (PAIRS, V, V), 1.0, 6.0, ((0, 8), (1, 4)), jnp.float32),
        "integrals": normal_values(keys[1], (ROWS, V), 0.08, 0.5, ((0, 8),), jnp.float32),
        "row_orbitals": with_ends(jax.random.randint(keys[2], (ROWS,), 0, V), jax.random.fold_in(keys[2], 1), 0, V - 1).astype(jnp.int32),
        "pair_orbitals": with_ends(jax.random.randint(keys[3], (PAIRS, 2), 0, NOCC), jax.random.fold_in(keys[3], 1), 0, NOCC - 1).astype(jnp.int32),
        "occupied_energy": jnp.clip(jax.random.uniform(keys[4], (NOCC,), jnp.float32, -2.0, -0.5), -2.0, -0.5),
        "virtual_energy": jnp.clip(jax.random.uniform(keys[5], (V,), jnp.float32, 0.5, 3.0), 0.5, 3.0),
    }


def reference(amplitudes, integrals, row_orbitals, pair_orbitals, occupied_energy, virtual_energy):
    indices = jnp.arange(PAIRS, dtype=jnp.int32)

    def one_pair(inputs):
        amp, orbs, index = inputs
        base = index // PAIR_DEV
        pair_energy = occupied_energy[orbs[0]] + occupied_energy[orbs[1]]
        total = jnp.zeros((V, V), jnp.float32)
        for offset in range(-(HOPS // 2), HOPS - HOPS // 2 + 1):
            source = ((base + offset) % N_BLK).astype(jnp.int32)
            start = (source * CH).astype(jnp.int32)
            block = lax.dynamic_slice_in_dim(integrals, start, CH, 0)
            rows = lax.dynamic_slice_in_dim(row_orbitals, start, CH, 0)
            row_energy = jnp.take(virtual_energy, rows)
            weighted = jnp.dot(block, amp, precision=lax.Precision.HIGHEST, preferred_element_type=jnp.float32)
            scaled = weighted / (row_energy[:, None] + virtual_energy[None, :] - pair_energy)
            total = total + jnp.dot(block.T, scaled, precision=lax.Precision.HIGHEST, preferred_element_type=jnp.float32)
        return total

    return lax.map(one_pair, (amplitudes, pair_orbitals, indices))
```

```python
import jax
import jax.numpy as jnp
from jax import lax
from jax.sharding import PartitionSpec as P

HOPS = 5
PREC = lax.Precision.HIGH


def fetch(block, axis, offset):
    n = lax.axis_size(axis)
    route = [((i + offset) % n, i) for i in range(n)]
    return lax.ppermute(block, axis, route)


def local(amplitudes, integrals, row_orbitals, pair_orbitals, occupied_energy, virtual_energy):
    width = virtual_energy.shape[0]
    quarter = width // lax.axis_size("vb")
    qstart = lax.axis_index("vb") * quarter
    row_energy = jnp.take(virtual_energy, row_orbitals, axis=0)
    pair_energy = (
        jnp.take(occupied_energy, pair_orbitals[:, 0], axis=0)
        + jnp.take(occupied_energy, pair_orbitals[:, 1], axis=0)
    )
    own_virtual = lax.dynamic_slice_in_dim(virtual_energy, qstart, quarter, 0)

    low = -(HOPS // 2)
    high = HOPS - HOPS // 2
    offsets = [0] + [o for k in range(1, high + 1) for o in (-k, k) if low <= o <= high and o != 0]
    window = []
    for o in offsets:
        if o == 0:
            window.append((integrals, row_energy))
        else:
            window.append((fetch(integrals, "blk", o), fetch(row_energy, "blk", o)))

    factors = lax.all_to_all(amplitudes, "vb", split_axis=2, concat_axis=1, tiled=True)

    total = None
    for block, energies in window:
        weighted = jnp.einsum(
            "rb,pba->rpa", block, factors, precision=PREC, preferred_element_type=jnp.float32
        )
        denom = (energies[:, None] + own_virtual[None, :])[:, None, :] - pair_energy[None, :, None]
        scaled = weighted / denom
        part = jnp.einsum(
            "rc,rpa->pca", block, scaled, precision=PREC, preferred_element_type=jnp.float32
        )
        total = part if total is None else total + part
    return lax.all_to_all(total, "vb", split_axis=1, concat_axis=2, tiled=True)


def solution(mesh):
    return jax.shard_map(
        local,
        mesh=mesh,
        in_specs=(P("blk", "vb", None), P("blk", None), P("blk"), P("blk", None), P(), P()),
        out_specs=P("blk", "vb", None),
        check_vma=False,
    )
```

```python
import jax
import jax.numpy as jnp
from jax import lax
from jax.sharding import PartitionSpec as P

HOPS = 5
PREC = lax.Precision.HIGH


def fetch(block, axis, offset):
    n = lax.axis_size(axis)
    route = [((i + offset) % n, i) for i in range(n)]
    return lax.ppermute(block, axis, route)


def roll_lanes(x, shift, axis):
    size = x.shape[axis]
    doubled = jnp.concatenate([x, x], axis=axis)
    return lax.dynamic_slice_in_dim(doubled, (size - shift) % size, size, axis)


def local(amplitudes, integrals, row_orbitals, pair_orbitals, occupied_energy, virtual_energy):
    width = virtual_energy.shape[0]
    nv = lax.axis_size("vb")
    quarter = width // nv
    q = lax.axis_index("vb")
    qstart = q * quarter
    row_energy = jnp.take(virtual_energy, row_orbitals, axis=0)
    pair_energy = (
        jnp.take(occupied_energy, pair_orbitals[:, 0], axis=0)
        + jnp.take(occupied_energy, pair_orbitals[:, 1], axis=0)
    )
    own_virtual = lax.dynamic_slice_in_dim(virtual_energy, qstart, quarter, 0)

    pieces = [lax.dynamic_slice_in_dim(amplitudes, qstart, quarter, 2)]
    for k in range(1, nv):
        dest_start = ((q + k) % nv) * quarter
        send = lax.dynamic_slice_in_dim(amplitudes, dest_start, quarter, 2)
        pieces.append(lax.ppermute(send, "vb", [(i, (i + k) % nv) for i in range(nv)]))

    reversed_cols = jnp.concatenate(
        [integrals[:, ((-k) % nv) * quarter:((-k) % nv + 1) * quarter] for k in range(nv)], axis=1
    )
    rotated = roll_lanes(reversed_cols, qstart, 1)

    low = -(HOPS // 2)
    high = HOPS - HOPS // 2
    offsets = [0] + [o for k in range(1, high + 1) for o in (-k, k) if low <= o <= high and o != 0]
    window = []
    for o in offsets:
        if o == 0:
            window.append((rotated, row_energy))
        else:
            window.append((fetch(rotated, "blk", o), fetch(row_energy, "blk", o)))

    scaled_blocks = []
    for block, energies in window:
        weighted = None
        for k in range(nv):
            part = jnp.einsum(
                "rb,pba->rpa",
                block[:, k * quarter:(k + 1) * quarter],
                pieces[k],
                precision=PREC,
                preferred_element_type=jnp.float32,
            )
            weighted = part if weighted is None else weighted + part
        denom = (energies[:, None] + own_virtual[None, :])[:, None, :] - pair_energy[None, :, None]
        scaled_blocks.append(weighted / denom)

    received = [None] * nv
    for k in list(range(1, nv)) + [0]:
        total = None
        for (block, _), scaled in zip(window, scaled_blocks):
            part = jnp.einsum(
                "rc,rpa->pca",
                block[:, k * quarter:(k + 1) * quarter],
                scaled,
                precision=PREC,
                preferred_element_type=jnp.float32,
            )
            total = part if total is None else total + part
        if k == 0:
            received[0] = total
        else:
            received[k] = lax.ppermute(total, "vb", [(i, (i - k) % nv) for i in range(nv)])
    gathered = jnp.concatenate(received, axis=2)
    return roll_lanes(gathered, qstart, 2)


def solution(mesh):
    return jax.shard_map(
        local,
        mesh=mesh,
        in_specs=(P("blk", "vb", None), P("blk", None), P("blk"), P("blk", None), P(), P()),
        out_specs=P("blk", "vb", None),
        check_vma=False,
    )
```

```python
import jax
import jax.numpy as jnp
from jax import lax
from jax.sharding import PartitionSpec as P

HOPS = 5
PREC = lax.Precision.HIGH


def roll_lanes(x, shift, axis):
    size = x.shape[axis]
    doubled = jnp.concatenate([x, x], axis=axis)
    return lax.dynamic_slice_in_dim(doubled, (size - shift) % size, size, axis)


def window_blocks(packed):
    nb = lax.axis_size("blk")
    even = range(0, nb, 2)
    core = lax.axis_index("blk") % 2

    def perm(x, pairs):
        return lax.ppermute(x, "blk", [(s % nb, t % nb) for s, t in pairs])

    a = perm(packed, [(d - 2, d) for d in even] + [(d + 3, d + 1) for d in even])
    b = perm(packed, [(d - 1, d) for d in even] + [(d + 2, d + 1) for d in even])
    c = perm(packed, [(d + 4, d + 1) for d in even])
    swap = [(d, d + 1) for d in even] + [(d + 1, d) for d in even]
    e = perm(packed, swap)
    f = perm(b, swap)
    g = perm(a, [(d + 1, d) for d in even])
    last = jnp.where(core == 0, g, c)
    return [packed, e, b, a, f, last]


def local(amplitudes, integrals, row_orbitals, pair_orbitals, occupied_energy, virtual_energy):
    assert HOPS == 5 and lax.axis_size("blk") % 2 == 0
    width = virtual_energy.shape[0]
    rows = integrals.shape[0]
    nv = lax.axis_size("vb")
    quarter = width // nv
    q = lax.axis_index("vb")
    qstart = q * quarter
    row_energy = jnp.take(virtual_energy, row_orbitals, axis=0)
    pair_energy = (
        jnp.take(occupied_energy, pair_orbitals[:, 0], axis=0)
        + jnp.take(occupied_energy, pair_orbitals[:, 1], axis=0)
    )
    own_virtual = lax.dynamic_slice_in_dim(virtual_energy, qstart, quarter, 0)

    pieces = [lax.dynamic_slice_in_dim(amplitudes, qstart, quarter, 2)]
    for k in range(1, nv):
        dest_start = ((q + k) % nv) * quarter
        send = lax.dynamic_slice_in_dim(amplitudes, dest_start, quarter, 2)
        pieces.append(lax.ppermute(send, "vb", [(i, (i + k) % nv) for i in range(nv)]))
    rest = jnp.concatenate(pieces[1:], axis=1)

    reversed_cols = jnp.concatenate(
        [integrals[:, ((-k) % nv) * quarter:((-k) % nv + 1) * quarter] for k in range(nv)], axis=1
    )
    rotated = roll_lanes(reversed_cols, qstart, 1)
    erows = -(-rows // width)
    erows_padded = -(-erows // 8) * 8
    energy_rows = jnp.pad(row_energy, (0, erows_padded * width - rows)).reshape(erows_padded, width)
    packed = jnp.concatenate([rotated, energy_rows], axis=0)

    remote = None
    scaled_blocks = []
    window = window_blocks(packed)
    for item in window:
        block = item[:rows]
        energies = item[rows:].reshape(-1)[:rows]
        weighted = jnp.einsum(
            "rb,pba->rpa", block[:, :quarter], pieces[0], precision=PREC, preferred_element_type=jnp.float32
        ) + jnp.einsum(
            "rb,pba->rpa", block[:, quarter:], rest, precision=PREC, preferred_element_type=jnp.float32
        )
        denom = (energies[:, None] + own_virtual[None, :])[:, None, :] - pair_energy[None, :, None]
        scaled = weighted / denom
        scaled_blocks.append((block, scaled))
        part = jnp.einsum(
            "rc,rpa->pca", block[:, quarter:], scaled, precision=PREC, preferred_element_type=jnp.float32
        )
        remote = part if remote is None else remote + part

    received = [None] * nv
    for k in range(1, nv):
        chunk = remote[:, (k - 1) * quarter:k * quarter]
        received[k] = lax.ppermute(chunk, "vb", [(i, (i - k) % nv) for i in range(nv)])
    own = None
    for block, scaled in scaled_blocks:
        part = jnp.einsum(
            "rc,rpa->pca", block[:, :quarter], scaled, precision=PREC, preferred_element_type=jnp.float32
        )
        own = part if own is None else own + part
    received[0] = own
    gathered = jnp.concatenate(received, axis=2)
    return roll_lanes(gathered, qstart, 2)


def solution(mesh):
    return jax.shard_map(
        local,
        mesh=mesh,
        in_specs=(P("blk", "vb", None), P("blk", None), P("blk"), P("blk", None), P(), P()),
        out_specs=P("blk", "vb", None),
        check_vma=False,
    )
```

```python
import jax
import jax.numpy as jnp
from jax import lax
from jax.sharding import PartitionSpec as P

HOPS = 5
PREC = lax.Precision.HIGH


def roll_lanes(x, shift, axis):
    size = x.shape[axis]
    doubled = jnp.concatenate([x, x], axis=axis)
    return lax.dynamic_slice_in_dim(doubled, (size - shift) % size, size, axis)


def window_blocks(packed):
    nb = lax.axis_size("blk")
    even = range(0, nb, 2)
    core = lax.axis_index("blk") % 2

    def perm(x, pairs):
        return lax.ppermute(x, "blk", [(s % nb, t % nb) for s, t in pairs])

    a = perm(packed, [(d - 2, d) for d in even] + [(d + 3, d + 1) for d in even])
    b = perm(packed, [(d - 1, d) for d in even] + [(d + 2, d + 1) for d in even])
    c = perm(packed, [(d + 4, d + 1) for d in even])
    swap = [(d, d + 1) for d in even] + [(d + 1, d) for d in even]
    e = perm(packed, swap)
    f = perm(b, swap)
    g = perm(a, [(d + 1, d) for d in even])
    last = jnp.where(core == 0, g, c)
    return [packed, e, b, a, f, last]


def local(amplitudes, integrals, row_orbitals, pair_orbitals, occupied_energy, virtual_energy):
    assert HOPS == 5 and lax.axis_size("blk") % 2 == 0
    width = virtual_energy.shape[0]
    rows = integrals.shape[0]
    nv = lax.axis_size("vb")
    quarter = width // nv
    q = lax.axis_index("vb")
    qstart = q * quarter
    row_energy = jnp.take(virtual_energy, row_orbitals, axis=0)
    pair_energy = (
        jnp.take(occupied_energy, pair_orbitals[:, 0], axis=0)
        + jnp.take(occupied_energy, pair_orbitals[:, 1], axis=0)
    )
    own_virtual = lax.dynamic_slice_in_dim(virtual_energy, qstart, quarter, 0)

    pieces = [lax.dynamic_slice_in_dim(amplitudes, qstart, quarter, 2)]
    for k in range(1, nv):
        dest_start = ((q + k) % nv) * quarter
        send = lax.dynamic_slice_in_dim(amplitudes, dest_start, quarter, 2)
        pieces.append(lax.ppermute(send, "vb", [(i, (i + k) % nv) for i in range(nv)]))
    rest = jnp.concatenate(pieces[1:], axis=1)

    reversed_cols = jnp.concatenate(
        [integrals[:, ((-k) % nv) * quarter:((-k) % nv + 1) * quarter] for k in range(nv)], axis=1
    )
    rotated = roll_lanes(reversed_cols, qstart, 1)
    erows = -(-rows // width)
    erows_padded = -(-erows // 8) * 8
    energy_rows = jnp.pad(row_energy, (0, erows_padded * width - rows)).reshape(erows_padded, width)
    packed = jnp.concatenate([rotated, energy_rows], axis=0)

    window = window_blocks(packed)
    scaled_blocks = []
    for item in window:
        block = item[:rows]
        energies = item[rows:].reshape(-1)[:rows]
        weighted = jnp.einsum(
            "rb,pba->rpa", block[:, :quarter], pieces[0], precision=PREC, preferred_element_type=jnp.float32
        ) + jnp.einsum(
            "rb,pba->rpa", block[:, quarter:], rest, precision=PREC, preferred_element_type=jnp.float32
        )
        denom = (energies[:, None] + own_virtual[None, :])[:, None, :] - pair_energy[None, :, None]
        scaled_blocks.append((block, weighted / denom))

    def density(cols, blocks):
        total = None
        for block, scaled in blocks:
            part = jnp.einsum(
                "rc,rpa->pca", block[:, cols], scaled, precision=PREC, preferred_element_type=jnp.float32
            )
            total = part if total is None else total + part
        return total

    early = density(slice(quarter, None), scaled_blocks[:-1])
    received = [None] * nv
    order = [k for k in range(1, nv) if k != nv // 2] + ([nv // 2] if nv > 1 else [])
    for k in order:
        chunk = early[:, (k - 1) * quarter:k * quarter] + density(
            slice(k * quarter, (k + 1) * quarter), scaled_blocks[-1:]
        )
        received[k] = lax.ppermute(chunk, "vb", [(i, (i - k) % nv) for i in range(nv)])
    received[0] = density(slice(0, quarter), scaled_blocks)
    gathered = jnp.concatenate(received, axis=2)
    return roll_lanes(gathered, qstart, 2)


def solution(mesh):
    return jax.shard_map(
        local,
        mesh=mesh,
        in_specs=(P("blk", "vb", None), P("blk", None), P("blk"), P("blk", None), P(), P()),
        out_specs=P("blk", "vb", None),
        check_vma=False,
    )
```

```python
import jax
import jax.numpy as jnp
from jax import lax
from jax.sharding import PartitionSpec as P

HOPS = 5
PREC = lax.Precision.HIGH


def roll_lanes(x, shift, axis):
    size = x.shape[axis]
    doubled = jnp.concatenate([x, x], axis=axis)
    return lax.dynamic_slice_in_dim(doubled, (size - shift) % size, size, axis)


def window_blocks(packed):
    nb = lax.axis_size("blk")
    even = range(0, nb, 2)
    core = lax.axis_index("blk") % 2

    def perm(x, pairs):
        return lax.ppermute(x, "blk", [(s % nb, t % nb) for s, t in pairs])

    a = perm(packed, [(d - 2, d) for d in even] + [(d + 3, d + 1) for d in even])
    b = perm(packed, [(d - 1, d) for d in even] + [(d + 2, d + 1) for d in even])
    c = perm(packed, [(d + 4, d + 1) for d in even])
    swap = [(d, d + 1) for d in even] + [(d + 1, d) for d in even]
    e = perm(packed, swap)
    f = perm(b, swap)
    g = perm(a, [(d + 1, d) for d in even])
    last = jnp.where(core == 0, g, c)
    return [packed, e, b, a, f, last]


def local(amplitudes, integrals, row_orbitals, pair_orbitals, occupied_energy, virtual_energy):
    assert HOPS == 5 and lax.axis_size("blk") % 2 == 0
    width = virtual_energy.shape[0]
    rows = integrals.shape[0]
    nv = lax.axis_size("vb")
    quarter = width // nv
    q = lax.axis_index("vb")
    qstart = q * quarter
    row_energy = jnp.take(virtual_energy, row_orbitals, axis=0)
    pair_energy = (
        jnp.take(occupied_energy, pair_orbitals[:, 0], axis=0)
        + jnp.take(occupied_energy, pair_orbitals[:, 1], axis=0)
    )
    own_virtual = lax.dynamic_slice_in_dim(virtual_energy, qstart, quarter, 0)

    pieces = [lax.dynamic_slice_in_dim(amplitudes, qstart, quarter, 2)]
    for k in range(1, nv):
        dest_start = ((q + k) % nv) * quarter
        send = lax.dynamic_slice_in_dim(amplitudes, dest_start, quarter, 2)
        pieces.append(lax.ppermute(send, "vb", [(i, (i + k) % nv) for i in range(nv)]))
    rest = jnp.concatenate(pieces[1:], axis=1)

    reversed_cols = jnp.concatenate(
        [integrals[:, ((-k) % nv) * quarter:((-k) % nv + 1) * quarter] for k in range(nv)], axis=1
    )
    rotated = roll_lanes(reversed_cols, qstart, 1)
    erows = -(-rows // width)
    erows_padded = -(-erows // 8) * 8
    energy_rows = jnp.pad(row_energy, (0, erows_padded * width - rows)).reshape(erows_padded, width)
    packed = jnp.concatenate([rotated, energy_rows], axis=0)

    window = window_blocks(packed)
    scaled_blocks = []
    for item in window:
        block = item[:rows]
        energies = item[rows:].reshape(-1)[:rows]
        weighted = jnp.einsum(
            "rb,pba->pra", block[:, :quarter], pieces[0], precision=PREC, preferred_element_type=jnp.float32
        ) + jnp.einsum(
            "rb,pba->pra", block[:, quarter:], rest, precision=PREC, preferred_element_type=jnp.float32
        )
        denom = (energies[:, None] + own_virtual[None, :])[None, :, :] - pair_energy[:, None, None]
        scaled_blocks.append((block, weighted / denom))

    def density(cols, pair):
        total = None
        for block, scaled in scaled_blocks:
            part = jnp.einsum(
                "rc,ra->ca", block[:, cols], scaled[pair], precision=PREC, preferred_element_type=jnp.float32
            )
            total = part if total is None else total + part
        return total

    npairs = amplitudes.shape[0]
    received = [[None] * npairs for _ in range(nv)]
    for p in range(npairs):
        remote = density(slice(quarter, None), p)
        for k in range(1, nv):
            chunk = remote[(k - 1) * quarter:k * quarter]
            received[k][p] = lax.ppermute(chunk, "vb", [(i, (i - k) % nv) for i in range(nv)])
        received[0][p] = density(slice(0, quarter), p)
    received = [jnp.stack(r) for r in received]
    gathered = jnp.concatenate(received, axis=2)
    return roll_lanes(gathered, qstart, 2)


def solution(mesh):
    return jax.shard_map(
        local,
        mesh=mesh,
        in_specs=(P("blk", "vb", None), P("blk", None), P("blk"), P("blk", None), P(), P()),
        out_specs=P("blk", "vb", None),
        check_vma=False,
    )
```

```python
import jax
import jax.numpy as jnp
from jax import lax
from jax.sharding import PartitionSpec as P


HOPS = 5
PREC = lax.Precision.HIGH


def roll_lanes(x, shift, axis):
    size = x.shape[axis]
    doubled = jnp.concatenate([x, x], axis=axis)
    return lax.dynamic_slice_in_dim(doubled, (size - shift) % size, size, axis)


def window_blocks(packed):
    nb = lax.axis_size("blk")
    even = range(0, nb, 2)
    core = lax.axis_index("blk") % 2

    def perm(x, pairs):
        return lax.ppermute(x, "blk", [(s % nb, t % nb) for s, t in pairs])

    a = perm(packed, [(d - 2, d) for d in even] + [(d + 3, d + 1) for d in even])
    b = perm(packed, [(d - 1, d) for d in even] + [(d + 2, d + 1) for d in even])
    c = perm(packed, [(d + 4, d + 1) for d in even])
    swap = [(d, d + 1) for d in even] + [(d + 1, d) for d in even]
    e = perm(packed, swap)
    f = perm(b, swap)
    g = perm(a, [(d + 1, d) for d in even])
    last = jnp.where(core == 0, g, c)
    return [packed, e, b, a, f, last]


def local(amplitudes, integrals, row_orbitals, pair_orbitals, occupied_energy, virtual_energy):
    assert HOPS == 5 and lax.axis_size("blk") % 2 == 0
    width = virtual_energy.shape[0]
    rows = integrals.shape[0]
    nv = lax.axis_size("vb")
    quarter = width // nv
    q = lax.axis_index("vb")
    qstart = q * quarter
    row_energy = jnp.take(virtual_energy, row_orbitals, axis=0)
    pair_energy = (
        jnp.take(occupied_energy, pair_orbitals[:, 0], axis=0)
        + jnp.take(occupied_energy, pair_orbitals[:, 1], axis=0)
    )
    own_virtual = lax.dynamic_slice_in_dim(virtual_energy, qstart, quarter, 0)

    pieces = [lax.dynamic_slice_in_dim(amplitudes, qstart, quarter, 2)]
    for k in range(1, nv):
        dest_start = ((q + k) % nv) * quarter
        send = lax.dynamic_slice_in_dim(amplitudes, dest_start, quarter, 2)
        pieces.append(lax.ppermute(send, "vb", [(i, (i + k) % nv) for i in range(nv)]))
    rest = jnp.concatenate(pieces[1:], axis=1)

    reversed_cols = jnp.concatenate(
        [integrals[:, ((-k) % nv) * quarter:((-k) % nv + 1) * quarter] for k in range(nv)], axis=1
    )
    rotated = roll_lanes(reversed_cols, qstart, 1)
    erows = -(-rows // width)
    erows_padded = -(-erows // 8) * 8
    energy_rows = jnp.pad(row_energy, (0, erows_padded * width - rows)).reshape(erows_padded, width)
    packed = jnp.concatenate([rotated, energy_rows], axis=0)

    window = [(item[:rows], item[rows:].reshape(-1)[:rows]) for item in window_blocks(packed)]

    npairs = amplitudes.shape[0]
    groups = [slice(0, npairs // 2), slice(npairs // 2, npairs)] if npairs > 1 else [slice(0, npairs)]
    received = [[] for _ in range(nv)]
    for group in groups:
      remote = None
      scaled_blocks = []
      for block, energies in window:
          weighted = jnp.einsum(
              "rb,pba->rpa", block[:, :quarter], pieces[0][group], precision=PREC,
              preferred_element_type=jnp.float32,
          ) + jnp.einsum(
              "rb,pba->rpa", block[:, quarter:], rest[group], precision=PREC,
              preferred_element_type=jnp.float32,
          )
          denom = (energies[:, None] + own_virtual[None, :])[:, None, :] - pair_energy[group][None, :, None]
          scaled = weighted / denom
          scaled_blocks.append((block, scaled))
          part = jnp.einsum(
              "rc,rpa->pca", block[:, quarter:], scaled, precision=PREC, preferred_element_type=jnp.float32
          )
          remote = part if remote is None else remote + part
      for k in range(1, nv):
          chunk = remote[:, (k - 1) * quarter:k * quarter]
          received[k].append(lax.ppermute(chunk, "vb", [(i, (i - k) % nv) for i in range(nv)]))
      own = None
      for block, scaled in scaled_blocks:
          part = jnp.einsum(
              "rc,rpa->pca", block[:, :quarter], scaled, precision=PREC, preferred_element_type=jnp.float32
          )
          own = part if own is None else own + part
      received[0].append(own)
    received = [jnp.concatenate(r, axis=0) for r in received]
    gathered = jnp.concatenate(received, axis=2)
    return roll_lanes(gathered, qstart, 2)


def solution(mesh):
    return jax.shard_map(
        local,
        mesh=mesh,
        in_specs=(P("blk", "vb", None), P("blk", None), P("blk"), P("blk", None), P(), P()),
        out_specs=P("blk", "vb", None),
        check_vma=False,
    )
```

```python
import jax
import jax.numpy as jnp
from jax import lax
from jax.sharding import PartitionSpec as P


HOPS = 5
PREC = lax.Precision.HIGH


def roll_lanes(x, shift, axis):
    size = x.shape[axis]
    doubled = jnp.concatenate([x, x], axis=axis)
    return lax.dynamic_slice_in_dim(doubled, (size - shift) % size, size, axis)


def window_blocks(packed):
    nb = lax.axis_size("blk")
    even = range(0, nb, 2)
    core = lax.axis_index("blk") % 2

    def perm(x, pairs):
        return lax.ppermute(x, "blk", [(s % nb, t % nb) for s, t in pairs])

    a = perm(packed, [(d - 2, d) for d in even] + [(d + 3, d + 1) for d in even])
    b = perm(packed, [(d - 1, d) for d in even] + [(d + 2, d + 1) for d in even])
    c = perm(packed, [(d + 4, d + 1) for d in even])
    swap = [(d, d + 1) for d in even] + [(d + 1, d) for d in even]
    e = perm(packed, swap)
    f = perm(b, swap)
    g = perm(a, [(d + 1, d) for d in even])
    last = jnp.where(core == 0, g, c)
    return [packed, e, b, a, f, last]


def local(amplitudes, integrals, row_orbitals, pair_orbitals, occupied_energy, virtual_energy):
    assert HOPS == 5 and lax.axis_size("blk") % 2 == 0
    width = virtual_energy.shape[0]
    rows = integrals.shape[0]
    nv = lax.axis_size("vb")
    quarter = width // nv
    q = lax.axis_index("vb")
    qstart = q * quarter
    row_energy = jnp.take(virtual_energy, row_orbitals, axis=0)
    pair_energy = (
        jnp.take(occupied_energy, pair_orbitals[:, 0], axis=0)
        + jnp.take(occupied_energy, pair_orbitals[:, 1], axis=0)
    )
    own_virtual = lax.dynamic_slice_in_dim(virtual_energy, qstart, quarter, 0)

    pieces = [lax.dynamic_slice_in_dim(amplitudes, qstart, quarter, 2)]
    for k in range(1, nv):
        dest_start = ((q + k) % nv) * quarter
        send = lax.dynamic_slice_in_dim(amplitudes, dest_start, quarter, 2)
        pieces.append(lax.ppermute(send, "vb", [(i, (i + k) % nv) for i in range(nv)]))
    rest = jnp.concatenate(pieces[1:], axis=1)

    reversed_cols = jnp.concatenate(
        [integrals[:, ((-k) % nv) * quarter:((-k) % nv + 1) * quarter] for k in range(nv)], axis=1
    )
    rotated = roll_lanes(reversed_cols, qstart, 1)
    erows = -(-rows // width)
    erows_padded = -(-erows // 8) * 8
    energy_rows = jnp.pad(row_energy, (0, erows_padded * width - rows)).reshape(erows_padded, width)
    packed = jnp.concatenate([rotated, energy_rows], axis=0)

    window = [(item[:rows], item[rows:].reshape(-1)[:rows]) for item in window_blocks(packed)]

    npairs = amplitudes.shape[0]
    head = max(1, npairs // 4)
    groups = [slice(0, head), slice(head, npairs)] if npairs > head else [slice(0, npairs)]
    received = [[] for _ in range(nv)]
    for group in groups:
      remote = None
      scaled_blocks = []
      for block, energies in window:
          weighted = jnp.einsum(
              "rb,pba->rpa", block[:, :quarter], pieces[0][group], precision=PREC,
              preferred_element_type=jnp.float32,
          ) + jnp.einsum(
              "rb,pba->rpa", block[:, quarter:], rest[group], precision=PREC,
              preferred_element_type=jnp.float32,
          )
          denom = (energies[:, None] + own_virtual[None, :])[:, None, :] - pair_energy[group][None, :, None]
          scaled = weighted / denom
          scaled_blocks.append((block, scaled))
          part = jnp.einsum(
              "rc,rpa->pca", block[:, quarter:], scaled, precision=PREC, preferred_element_type=jnp.float32
          )
          remote = part if remote is None else remote + part
      for k in range(1, nv):
          chunk = remote[:, (k - 1) * quarter:k * quarter]
          received[k].append(lax.ppermute(chunk, "vb", [(i, (i - k) % nv) for i in range(nv)]))
      own = None
      for block, scaled in scaled_blocks:
          part = jnp.einsum(
              "rc,rpa->pca", block[:, :quarter], scaled, precision=PREC, preferred_element_type=jnp.float32
          )
          own = part if own is None else own + part
      received[0].append(own)
    received = [jnp.concatenate(r, axis=0) for r in received]
    out = jnp.zeros(received[0].shape[:2] + (width,), received[0].dtype)
    for k in range(nv):
        out = lax.dynamic_update_slice_in_dim(out, received[k], ((q + k) % nv) * quarter, 2)
    return out


def solution(mesh):
    return jax.shard_map(
        local,
        mesh=mesh,
        in_specs=(P("blk", "vb", None), P("blk", None), P("blk"), P("blk", None), P(), P()),
        out_specs=P("blk", "vb", None),
        check_vma=False,
    )
```

```python
import jax
import jax.numpy as jnp
from jax import lax
from jax.sharding import PartitionSpec as P

HOPS = 5
PREC = lax.Precision.HIGH


def roll_lanes(x, shift, axis):
    size = x.shape[axis]
    doubled = jnp.concatenate([x, x], axis=axis)
    return lax.dynamic_slice_in_dim(doubled, (size - shift) % size, size, axis)


def window_blocks(packed):
    nb = lax.axis_size("blk")
    even = range(0, nb, 2)
    core = lax.axis_index("blk") % 2

    def perm(x, pairs):
        return lax.ppermute(x, "blk", [(s % nb, t % nb) for s, t in pairs])

    a = perm(packed, [(d - 2, d) for d in even] + [(d + 3, d + 1) for d in even])
    b = perm(packed, [(d - 1, d) for d in even] + [(d + 2, d + 1) for d in even])
    c = perm(b, [(d + 3, d + 1) for d in even])
    swap = [(d, d + 1) for d in even] + [(d + 1, d) for d in even]
    e = perm(packed, swap)
    f = perm(b, swap)
    g = perm(a, [(d + 1, d) for d in even])
    last = jnp.where(core == 0, g, c)
    return [packed, e, b, a, f, last]


def local(amplitudes, integrals, row_orbitals, pair_orbitals, occupied_energy, virtual_energy):
    assert HOPS == 5 and lax.axis_size("blk") % 2 == 0
    width = virtual_energy.shape[0]
    rows = integrals.shape[0]
    nv = lax.axis_size("vb")
    quarter = width // nv
    q = lax.axis_index("vb")
    qstart = q * quarter
    row_energy = jnp.take(virtual_energy, row_orbitals, axis=0)
    pair_energy = (
        jnp.take(occupied_energy, pair_orbitals[:, 0], axis=0)
        + jnp.take(occupied_energy, pair_orbitals[:, 1], axis=0)
    )
    own_virtual = lax.dynamic_slice_in_dim(virtual_energy, qstart, quarter, 0)

    pieces = [lax.dynamic_slice_in_dim(amplitudes, qstart, quarter, 2)]
    for k in range(1, nv):
        dest_start = ((q + k) % nv) * quarter
        send = lax.dynamic_slice_in_dim(amplitudes, dest_start, quarter, 2)
        pieces.append(lax.ppermute(send, "vb", [(i, (i + k) % nv) for i in range(nv)]))
    rest = jnp.concatenate(pieces[1:], axis=1)

    reversed_cols = jnp.concatenate(
        [integrals[:, ((-k) % nv) * quarter:((-k) % nv + 1) * quarter] for k in range(nv)], axis=1
    )
    rotated = roll_lanes(reversed_cols, qstart, 1)
    erows = -(-rows // width)
    erows_padded = -(-erows // 8) * 8
    energy_rows = jnp.pad(row_energy, (0, erows_padded * width - rows)).reshape(erows_padded, width)
    packed = jnp.concatenate([rotated, energy_rows], axis=0)

    remote = None
    scaled_blocks = []
    window = window_blocks(packed)
    for item in window:
        block = item[:rows]
        energies = item[rows:].reshape(-1)[:rows]
        weighted = jnp.einsum(
            "rb,pba->rpa", block[:, :quarter], pieces[0], precision=PREC, preferred_element_type=jnp.float32
        ) + jnp.einsum(
            "rb,pba->rpa", block[:, quarter:], rest, precision=PREC, preferred_element_type=jnp.float32
        )
        denom = (energies[:, None] + own_virtual[None, :])[:, None, :] - pair_energy[None, :, None]
        scaled = weighted / denom
        scaled_blocks.append((block, scaled))
        part = jnp.einsum(
            "rc,rpa->pca", block[:, quarter:], scaled, precision=PREC, preferred_element_type=jnp.float32
        )
        remote = part if remote is None else remote + part

    received = [None] * nv
    for k in range(1, nv):
        chunk = remote[:, (k - 1) * quarter:k * quarter]
        received[k] = lax.ppermute(chunk, "vb", [(i, (i - k) % nv) for i in range(nv)])
    own = None
    for block, scaled in scaled_blocks:
        part = jnp.einsum(
            "rc,rpa->pca", block[:, :quarter], scaled, precision=PREC, preferred_element_type=jnp.float32
        )
        own = part if own is None else own + part
    received[0] = own
    gathered = jnp.concatenate(received, axis=2)
    return roll_lanes(gathered, qstart, 2)


def solution(mesh):
    return jax.shard_map(
        local,
        mesh=mesh,
        in_specs=(P("blk", "vb", None), P("blk", None), P("blk"), P("blk", None), P(), P()),
        out_specs=P("blk", "vb", None),
        check_vma=False,
    )
```

```python
import jax
import jax.numpy as jnp
from jax import lax
from jax.sharding import PartitionSpec as P

HOPS = 5
PREC = lax.Precision.HIGH


def roll_lanes(x, shift, axis):
    size = x.shape[axis]
    doubled = jnp.concatenate([x, x], axis=axis)
    return lax.dynamic_slice_in_dim(doubled, (size - shift) % size, size, axis)


def window_blocks(packed):
    nb = lax.axis_size("blk")
    even = range(0, nb, 2)
    core = lax.axis_index("blk") % 2

    def perm(x, pairs):
        return lax.ppermute(x, "blk", [(s % nb, t % nb) for s, t in pairs])

    a = perm(packed, [(d - 2, d) for d in even] + [(d + 3, d + 1) for d in even])
    b = perm(packed, [(d - 1, d) for d in even] + [(d + 2, d + 1) for d in even])
    c = perm(b, [(d + 3, d + 1) for d in even])
    swap = [(d, d + 1) for d in even] + [(d + 1, d) for d in even]
    e = perm(packed, swap)
    f = perm(b, swap)
    g = perm(a, [(d + 1, d) for d in even])
    last = jnp.where(core == 0, g, c)
    return [packed, e, b, a, f, last]


def local(amplitudes, integrals, row_orbitals, pair_orbitals, occupied_energy, virtual_energy):
    assert HOPS == 5 and lax.axis_size("blk") % 2 == 0
    width = virtual_energy.shape[0]
    rows = integrals.shape[0]
    nv = lax.axis_size("vb")
    quarter = width // nv
    q = lax.axis_index("vb")
    qstart = q * quarter
    row_energy = jnp.take(virtual_energy, row_orbitals, axis=0)
    pair_energy = (
        jnp.take(occupied_energy, pair_orbitals[:, 0], axis=0)
        + jnp.take(occupied_energy, pair_orbitals[:, 1], axis=0)
    )
    own_virtual = lax.dynamic_slice_in_dim(virtual_energy, qstart, quarter, 0)

    pieces = [lax.dynamic_slice_in_dim(amplitudes, qstart, quarter, 2)]
    for k in range(1, nv):
        dest_start = ((q + k) % nv) * quarter
        send = lax.dynamic_slice_in_dim(amplitudes, dest_start, quarter, 2)
        pieces.append(lax.ppermute(send, "vb", [(i, (i + k) % nv) for i in range(nv)]))
    rest = jnp.concatenate(pieces[1:], axis=1)

    reversed_cols = jnp.concatenate(
        [integrals[:, ((-k) % nv) * quarter:((-k) % nv + 1) * quarter] for k in range(nv)], axis=1
    )
    rotated = roll_lanes(reversed_cols, qstart, 1)
    erows = -(-rows // width)
    erows_padded = -(-erows // 8) * 8
    energy_rows = jnp.pad(row_energy, (0, erows_padded * width - rows)).reshape(erows_padded, width)
    packed = jnp.concatenate([rotated, energy_rows], axis=0)

    window = [(item[:rows], item[rows:].reshape(-1)[:rows]) for item in window_blocks(packed)]

    def scaled_of(block, energies):
        weighted = jnp.einsum(
            "rb,pba->rpa", block[:, :quarter], pieces[0], precision=PREC, preferred_element_type=jnp.float32
        ) + jnp.einsum(
            "rb,pba->rpa", block[:, quarter:], rest, precision=PREC, preferred_element_type=jnp.float32
        )
        denom = (energies[:, None] + own_virtual[None, :])[:, None, :] - pair_energy[None, :, None]
        return weighted / denom

    def density(cols, blocks):
        total = None
        for block, scaled in blocks:
            part = jnp.einsum(
                "rc,rpa->pca", block[:, cols], scaled, precision=PREC, preferred_element_type=jnp.float32
            )
            total = part if total is None else total + part
        return total

    first = [(block, scaled_of(block, energies)) for block, energies in window[:4]]
    remote_first = density(slice(quarter, None), first)
    own_first = density(slice(0, quarter), first)
    late, remote_first, own_first = lax.optimization_barrier((window[4:], remote_first, own_first))
    last = [(block, scaled_of(block, energies)) for block, energies in late]
    remote = remote_first + density(slice(quarter, None), last)
    received = [None] * nv
    for k in range(1, nv):
        chunk = remote[:, (k - 1) * quarter:k * quarter]
        received[k] = lax.ppermute(chunk, "vb", [(i, (i - k) % nv) for i in range(nv)])
    received[0] = own_first + density(slice(0, quarter), last)
    gathered = jnp.concatenate(received, axis=2)
    return roll_lanes(gathered, qstart, 2)


def solution(mesh):
    return jax.shard_map(
        local,
        mesh=mesh,
        in_specs=(P("blk", "vb", None), P("blk", None), P("blk"), P("blk", None), P(), P()),
        out_specs=P("blk", "vb", None),
        check_vma=False,
    )
```

```python
import jax
import jax.numpy as jnp
from jax import lax
from jax.sharding import PartitionSpec as P

HOPS = 5
PREC = lax.Precision.HIGH


def roll_lanes(x, shift, axis):
    size = x.shape[axis]
    doubled = jnp.concatenate([x, x], axis=axis)
    return lax.dynamic_slice_in_dim(doubled, (size - shift) % size, size, axis)


def window_blocks(packed):
    nb = lax.axis_size("blk")
    even = range(0, nb, 2)
    core = lax.axis_index("blk") % 2

    def perm(x, pairs):
        return lax.ppermute(x, "blk", [(s % nb, t % nb) for s, t in pairs])

    a = perm(packed, [(d - 2, d) for d in even] + [(d + 3, d + 1) for d in even])
    b = perm(packed, [(d - 1, d) for d in even] + [(d + 2, d + 1) for d in even])
    c = perm(b, [(d + 3, d + 1) for d in even])
    swap = [(d, d + 1) for d in even] + [(d + 1, d) for d in even]
    e = perm(packed, swap)
    f = perm(b, swap)
    g = perm(a, [(d + 1, d) for d in even])
    last = jnp.where(core == 0, g, c)
    return [packed, e, b, a, f, last]


def local(amplitudes, integrals, row_orbitals, pair_orbitals, occupied_energy, virtual_energy):
    assert HOPS == 5 and lax.axis_size("blk") % 2 == 0
    width = virtual_energy.shape[0]
    rows = integrals.shape[0]
    nv = lax.axis_size("vb")
    quarter = width // nv
    q = lax.axis_index("vb")
    qstart = q * quarter
    row_energy = jnp.take(virtual_energy, row_orbitals, axis=0)
    pair_energy = (
        jnp.take(occupied_energy, pair_orbitals[:, 0], axis=0)
        + jnp.take(occupied_energy, pair_orbitals[:, 1], axis=0)
    )
    own_virtual = lax.dynamic_slice_in_dim(virtual_energy, qstart, quarter, 0)

    pieces = [lax.dynamic_slice_in_dim(amplitudes, qstart, quarter, 2)]
    for k in range(1, nv):
        dest_start = ((q + k) % nv) * quarter
        send = lax.dynamic_slice_in_dim(amplitudes, dest_start, quarter, 2)
        pieces.append(lax.ppermute(send, "vb", [(i, (i + k) % nv) for i in range(nv)]))
    rest = jnp.concatenate(pieces[1:], axis=1)

    reversed_cols = jnp.concatenate(
        [integrals[:, ((-k) % nv) * quarter:((-k) % nv + 1) * quarter] for k in range(nv)], axis=1
    )
    rotated = roll_lanes(reversed_cols, qstart, 1)
    erows = -(-rows // width)
    erows_padded = -(-erows // 8) * 8
    energy_rows = jnp.pad(row_energy, (0, erows_padded * width - rows)).reshape(erows_padded, width)
    packed = jnp.concatenate([rotated, energy_rows], axis=0)

    window = [(item[:rows], item[rows:].reshape(-1)[:rows]) for item in window_blocks(packed)]

    def scaled_of(block, energies):
        weighted = jnp.einsum(
            "rb,pba->rpa", block[:, :quarter], pieces[0], precision=PREC, preferred_element_type=jnp.float32
        ) + jnp.einsum(
            "rb,pba->rpa", block[:, quarter:], rest, precision=PREC, preferred_element_type=jnp.float32
        )
        denom = (energies[:, None] + own_virtual[None, :])[:, None, :] - pair_energy[None, :, None]
        return weighted / denom

    def density(cols, blocks):
        total = None
        for block, scaled in blocks:
            part = jnp.einsum(
                "rc,rpa->pca", block[:, cols], scaled, precision=PREC, preferred_element_type=jnp.float32
            )
            total = part if total is None else total + part
        return total

    early_blocks = [window[0], window[2], window[3]]
    late_blocks = [window[1], window[4], window[5]]
    first = [(block, scaled_of(block, energies)) for block, energies in early_blocks]
    remote_first = density(slice(quarter, None), first)
    own_first = density(slice(0, quarter), first)
    late, remote_first, own_first = lax.optimization_barrier((late_blocks, remote_first, own_first))
    last = [(block, scaled_of(block, energies)) for block, energies in late]
    remote = remote_first + density(slice(quarter, None), last)
    received = [None] * nv
    for k in range(1, nv):
        chunk = remote[:, (k - 1) * quarter:k * quarter]
        received[k] = lax.ppermute(chunk, "vb", [(i, (i - k) % nv) for i in range(nv)])
    received[0] = own_first + density(slice(0, quarter), last)
    gathered = jnp.concatenate(received, axis=2)
    return roll_lanes(gathered, qstart, 2)


def solution(mesh):
    return jax.shard_map(
        local,
        mesh=mesh,
        in_specs=(P("blk", "vb", None), P("blk", None), P("blk"), P("blk", None), P(), P()),
        out_specs=P("blk", "vb", None),
        check_vma=False,
    )
```

```python
import jax
import jax.numpy as jnp
from jax import lax
from jax.sharding import PartitionSpec as P

HOPS = 5
PREC = lax.Precision.HIGH


def roll_lanes(x, shift, axis):
    size = x.shape[axis]
    doubled = jnp.concatenate([x, x], axis=axis)
    return lax.dynamic_slice_in_dim(doubled, (size - shift) % size, size, axis)


def window_blocks(packed):
    nb = lax.axis_size("blk")
    even = range(0, nb, 2)
    core = lax.axis_index("blk") % 2

    def perm(x, pairs):
        return lax.ppermute(x, "blk", [(s % nb, t % nb) for s, t in pairs])

    a = perm(packed, [(d - 2, d) for d in even] + [(d + 3, d + 1) for d in even])
    b = perm(packed, [(d - 1, d) for d in even] + [(d + 2, d + 1) for d in even])
    c = perm(b, [(d + 3, d + 1) for d in even])
    swap = [(d, d + 1) for d in even] + [(d + 1, d) for d in even]
    e = perm(packed, swap)
    f = perm(b, swap)
    g = perm(a, [(d + 1, d) for d in even])
    last = jnp.where(core == 0, g, c)
    return [packed, e, b, a, f, last]


def local(amplitudes, integrals, row_orbitals, pair_orbitals, occupied_energy, virtual_energy):
    assert HOPS == 5 and lax.axis_size("blk") % 2 == 0
    width = virtual_energy.shape[0]
    rows = integrals.shape[0]
    nv = lax.axis_size("vb")
    quarter = width // nv
    q = lax.axis_index("vb")
    qstart = q * quarter
    row_energy = jnp.take(virtual_energy, row_orbitals, axis=0)
    pair_energy = (
        jnp.take(occupied_energy, pair_orbitals[:, 0], axis=0)
        + jnp.take(occupied_energy, pair_orbitals[:, 1], axis=0)
    )
    own_virtual = lax.dynamic_slice_in_dim(virtual_energy, qstart, quarter, 0)

    pieces = [lax.dynamic_slice_in_dim(amplitudes, qstart, quarter, 2)]
    for k in range(1, nv):
        dest_start = ((q + k) % nv) * quarter
        send = lax.dynamic_slice_in_dim(amplitudes, dest_start, quarter, 2)
        pieces.append(lax.ppermute(send, "vb", [(i, (i + k) % nv) for i in range(nv)]))
    rest = jnp.concatenate(pieces[1:], axis=1)

    reversed_cols = jnp.concatenate(
        [integrals[:, ((-k) % nv) * quarter:((-k) % nv + 1) * quarter] for k in range(nv)], axis=1
    )
    rotated = roll_lanes(reversed_cols, qstart, 1)
    erows = -(-rows // width)
    erows_padded = -(-erows // 8) * 8
    energy_rows = jnp.pad(row_energy, (0, erows_padded * width - rows)).reshape(erows_padded, width)
    packed = jnp.concatenate([rotated, energy_rows], axis=0)

    remote = None
    scaled_blocks = []
    window = window_blocks(packed)
    for item in window:
        block = item[:rows]
        energies = item[rows:].reshape(-1)[:rows]
        weighted = jnp.einsum(
            "rb,pba->rpa", block[:, :quarter], pieces[0], precision=PREC, preferred_element_type=jnp.float32
        ) + jnp.einsum(
            "rb,pba->rpa", block[:, quarter:], rest, precision=PREC, preferred_element_type=jnp.float32
        )
        denom = (energies[:, None] + own_virtual[None, :])[:, None, :] - pair_energy[None, :, None]
        scaled = weighted / denom
        scaled_blocks.append((block, scaled))
        part = jnp.einsum(
            "rc,rpa->pca", block[:, quarter:], scaled, precision=PREC, preferred_element_type=jnp.float32
        )
        remote = part if remote is None else remote + part

    received = [None] * nv
    for k in range(1, nv):
        chunk = remote[:, (k - 1) * quarter:k * quarter]
        received[k] = lax.ppermute(chunk, "vb", [(i, (i - k) % nv) for i in range(nv)])
    own = None
    for block, scaled in scaled_blocks:
        part = jnp.einsum(
            "rc,rpa->pca", block[:, :quarter], scaled, precision=PREC, preferred_element_type=jnp.float32
        )
        own = part if own is None else own + part
    received[0] = own
    out = jnp.zeros(received[0].shape[:2] + (width,), received[0].dtype)
    for k in range(nv):
        out = lax.dynamic_update_slice_in_dim(out, received[k], ((q + k) % nv) * quarter, 2)
    return out


def solution(mesh):
    return jax.shard_map(
        local,
        mesh=mesh,
        in_specs=(P("blk", "vb", None), P("blk", None), P("blk"), P("blk", None), P(), P()),
        out_specs=P("blk", "vb", None),
        check_vma=False,
    )
```

```python
import jax
import jax.numpy as jnp
from jax import lax
from jax.experimental.layout import Layout, with_layout_constraint
from jax.sharding import PartitionSpec as P

HOPS = 5
PREC = lax.Precision.HIGH


def roll_lanes(x, shift, axis):
    size = x.shape[axis]
    doubled = jnp.concatenate([x, x], axis=axis)
    return lax.dynamic_slice_in_dim(doubled, (size - shift) % size, size, axis)


def window_blocks(packed):
    nb = lax.axis_size("blk")
    even = range(0, nb, 2)
    core = lax.axis_index("blk") % 2

    def perm(x, pairs):
        return lax.ppermute(x, "blk", [(s % nb, t % nb) for s, t in pairs])

    a = perm(packed, [(d - 2, d) for d in even] + [(d + 3, d + 1) for d in even])
    b = perm(packed, [(d - 1, d) for d in even] + [(d + 2, d + 1) for d in even])
    c = perm(b, [(d + 3, d + 1) for d in even])
    swap = [(d, d + 1) for d in even] + [(d + 1, d) for d in even]
    e = perm(packed, swap)
    f = perm(b, swap)
    g = perm(a, [(d + 1, d) for d in even])
    last = jnp.where(core == 0, g, c)
    return [packed, e, b, a, f, last]


def local(amplitudes, integrals, row_orbitals, pair_orbitals, occupied_energy, virtual_energy):
    assert HOPS == 5 and lax.axis_size("blk") % 2 == 0
    width = virtual_energy.shape[0]
    rows = integrals.shape[0]
    nv = lax.axis_size("vb")
    quarter = width // nv
    q = lax.axis_index("vb")
    qstart = q * quarter
    row_energy = jnp.take(virtual_energy, row_orbitals, axis=0)
    pair_energy = (
        jnp.take(occupied_energy, pair_orbitals[:, 0], axis=0)
        + jnp.take(occupied_energy, pair_orbitals[:, 1], axis=0)
    )
    own_virtual = lax.dynamic_slice_in_dim(virtual_energy, qstart, quarter, 0)

    pieces = [lax.dynamic_slice_in_dim(amplitudes, qstart, quarter, 2)]
    for k in range(1, nv):
        dest_start = ((q + k) % nv) * quarter
        send = lax.dynamic_slice_in_dim(amplitudes, dest_start, quarter, 2)
        pieces.append(lax.ppermute(send, "vb", [(i, (i + k) % nv) for i in range(nv)]))
    rest = jnp.concatenate(pieces[1:], axis=1)

    reversed_cols = jnp.concatenate(
        [integrals[:, ((-k) % nv) * quarter:((-k) % nv + 1) * quarter] for k in range(nv)], axis=1
    )
    rotated = roll_lanes(reversed_cols, qstart, 1)
    erows = -(-rows // width)
    erows_padded = -(-erows // 8) * 8
    energy_rows = jnp.pad(row_energy, (0, erows_padded * width - rows)).reshape(erows_padded, width)
    packed = jnp.concatenate([rotated, energy_rows], axis=0)

    remote = None
    scaled_blocks = []
    window = window_blocks(packed)
    for item in window:
        block = item[:rows]
        energies = item[rows:].reshape(-1)[:rows]
        weighted = jnp.einsum(
            "rb,pba->rpa", block[:, :quarter], pieces[0], precision=PREC, preferred_element_type=jnp.float32
        ) + jnp.einsum(
            "rb,pba->rpa", block[:, quarter:], rest, precision=PREC, preferred_element_type=jnp.float32
        )
        denom = (energies[:, None] + own_virtual[None, :])[:, None, :] - pair_energy[None, :, None]
        scaled = weighted / denom
        scaled_blocks.append((block, scaled))
        part = jnp.einsum(
            "rc,rpa->pca", block[:, quarter:], scaled, precision=PREC, preferred_element_type=jnp.float32
        )
        remote = part if remote is None else remote + part
    remote = with_layout_constraint(remote, Layout(major_to_minor=(0, 1, 2)))

    received = [None] * nv
    for k in range(1, nv):
        chunk = remote[:, (k - 1) * quarter:k * quarter]
        received[k] = lax.ppermute(chunk, "vb", [(i, (i - k) % nv) for i in range(nv)])
    own = None
    for block, scaled in scaled_blocks:
        part = jnp.einsum(
            "rc,rpa->pca", block[:, :quarter], scaled, precision=PREC, preferred_element_type=jnp.float32
        )
        own = part if own is None else own + part
    received[0] = with_layout_constraint(own, Layout(major_to_minor=(0, 1, 2)))
    gathered = jnp.concatenate(received, axis=2)
    return roll_lanes(gathered, qstart, 2)


def solution(mesh):
    return jax.shard_map(
        local,
        mesh=mesh,
        in_specs=(P("blk", "vb", None), P("blk", None), P("blk"), P("blk", None), P(), P()),
        out_specs=P("blk", "vb", None),
        check_vma=False,
    )
```

```python
import jax
import jax.numpy as jnp
from jax import lax
from jax.experimental.layout import Layout, with_layout_constraint
from jax.sharding import PartitionSpec as P

HOPS = 5
PREC = lax.Precision.HIGH


def roll_lanes(x, shift, axis):
    size = x.shape[axis]
    doubled = jnp.concatenate([x, x], axis=axis)
    return lax.dynamic_slice_in_dim(doubled, (size - shift) % size, size, axis)


def window_blocks(packed):
    nb = lax.axis_size("blk")
    even = range(0, nb, 2)
    core = lax.axis_index("blk") % 2

    def perm(x, pairs):
        return lax.ppermute(x, "blk", [(s % nb, t % nb) for s, t in pairs])

    a = perm(packed, [(d - 2, d) for d in even] + [(d + 3, d + 1) for d in even])
    b = perm(packed, [(d - 1, d) for d in even] + [(d + 2, d + 1) for d in even])
    c = perm(b, [(d + 3, d + 1) for d in even])
    swap = [(d, d + 1) for d in even] + [(d + 1, d) for d in even]
    e = perm(packed, swap)
    f = perm(b, swap)
    g = perm(a, [(d + 1, d) for d in even])
    last = jnp.where(core == 0, g, c)
    return [packed, e, b, a, f, last]


def local(amplitudes, integrals, row_orbitals, pair_orbitals, occupied_energy, virtual_energy):
    assert HOPS == 5 and lax.axis_size("blk") % 2 == 0
    width = virtual_energy.shape[0]
    rows = integrals.shape[0]
    nv = lax.axis_size("vb")
    quarter = width // nv
    q = lax.axis_index("vb")
    qstart = q * quarter
    row_energy = jnp.take(virtual_energy, row_orbitals, axis=0)
    pair_energy = (
        jnp.take(occupied_energy, pair_orbitals[:, 0], axis=0)
        + jnp.take(occupied_energy, pair_orbitals[:, 1], axis=0)
    )
    own_virtual = lax.dynamic_slice_in_dim(virtual_energy, qstart, quarter, 0)

    pieces = [lax.dynamic_slice_in_dim(amplitudes, qstart, quarter, 2)]
    for k in range(1, nv):
        dest_start = ((q + k) % nv) * quarter
        send = lax.dynamic_slice_in_dim(amplitudes, dest_start, quarter, 2)
        pieces.append(lax.ppermute(send, "vb", [(i, (i + k) % nv) for i in range(nv)]))
    rest = jnp.concatenate(pieces[1:], axis=1)

    reversed_cols = jnp.concatenate(
        [integrals[:, ((-k) % nv) * quarter:((-k) % nv + 1) * quarter] for k in range(nv)], axis=1
    )
    rotated = roll_lanes(reversed_cols, qstart, 1)
    erows = -(-rows // width)
    erows_padded = -(-erows // 8) * 8
    energy_rows = jnp.pad(row_energy, (0, erows_padded * width - rows)).reshape(erows_padded, width)
    packed = jnp.concatenate([rotated, energy_rows], axis=0)

    remote = None
    scaled_blocks = []
    window = window_blocks(packed)
    for item in window:
        block = item[:rows]
        energies = item[rows:].reshape(-1)[:rows]
        weighted = jnp.einsum(
            "rb,pba->rpa", block[:, :quarter], pieces[0], precision=PREC, preferred_element_type=jnp.float32
        ) + jnp.einsum(
            "rb,pba->rpa", block[:, quarter:], rest, precision=PREC, preferred_element_type=jnp.float32
        )
        denom = (energies[:, None] + own_virtual[None, :])[:, None, :] - pair_energy[None, :, None]
        scaled = weighted / denom
        scaled_blocks.append((block, scaled))
        part = jnp.einsum(
            "rc,rpa->pca", block[:, quarter:], scaled, precision=PREC, preferred_element_type=jnp.float32
        )
        remote = part if remote is None else remote + part
    remote = with_layout_constraint(remote, Layout(major_to_minor=(0, 1, 2)))

    received = [None] * nv
    for k in range(1, nv):
        chunk = remote[:, (k - 1) * quarter:k * quarter]
        received[k] = lax.ppermute(chunk, "vb", [(i, (i - k) % nv) for i in range(nv)])
    own = None
    for block, scaled in scaled_blocks:
        part = jnp.einsum(
            "rc,rpa->pca", block[:, :quarter], scaled, precision=PREC, preferred_element_type=jnp.float32
        )
        own = part if own is None else own + part
    received[0] = with_layout_constraint(own, Layout(major_to_minor=(0, 1, 2)))
    out = jnp.zeros(received[0].shape[:2] + (width,), received[0].dtype)
    for k in range(nv):
        out = lax.dynamic_update_slice_in_dim(out, received[k], ((q + k) % nv) * quarter, 2)
    return out


def solution(mesh):
    return jax.shard_map(
        local,
        mesh=mesh,
        in_specs=(P("blk", "vb", None), P("blk", None), P("blk"), P("blk", None), P(), P()),
        out_specs=P("blk", "vb", None),
        check_vma=False,
    )
```

```python
import jax
import jax.numpy as jnp
from jax import lax
from jax.experimental.layout import Layout, with_layout_constraint
from jax.sharding import PartitionSpec as P

HOPS = 5
PREC = lax.Precision.HIGH


def roll_lanes(x, shift, axis):
    size = x.shape[axis]
    doubled = jnp.concatenate([x, x], axis=axis)
    return lax.dynamic_slice_in_dim(doubled, (size - shift) % size, size, axis)


def window_blocks(packed):
    nb = lax.axis_size("blk")
    even = range(0, nb, 2)
    core = lax.axis_index("blk") % 2

    def perm(x, pairs):
        return lax.ppermute(x, "blk", [(s % nb, t % nb) for s, t in pairs])

    a = perm(packed, [(d - 2, d) for d in even] + [(d + 3, d + 1) for d in even])
    b = perm(packed, [(d - 1, d) for d in even] + [(d + 2, d + 1) for d in even])
    c = perm(b, [(d + 3, d + 1) for d in even])
    swap = [(d, d + 1) for d in even] + [(d + 1, d) for d in even]
    e = perm(packed, swap)
    f = perm(b, swap)
    g = perm(a, [(d + 1, d) for d in even])
    last = jnp.where(core == 0, g, c)
    return [packed, e, b, a, f, last]


def local(amplitudes, integrals, row_orbitals, pair_orbitals, occupied_energy, virtual_energy):
    assert HOPS == 5 and lax.axis_size("blk") % 2 == 0
    width = virtual_energy.shape[0]
    rows = integrals.shape[0]
    nv = lax.axis_size("vb")
    quarter = width // nv
    q = lax.axis_index("vb")
    qstart = q * quarter
    row_energy = jnp.take(virtual_energy, row_orbitals, axis=0)
    pair_energy = (
        jnp.take(occupied_energy, pair_orbitals[:, 0], axis=0)
        + jnp.take(occupied_energy, pair_orbitals[:, 1], axis=0)
    )
    own_virtual = lax.dynamic_slice_in_dim(virtual_energy, qstart, quarter, 0)

    pieces = [lax.dynamic_slice_in_dim(amplitudes, qstart, quarter, 2)]
    for k in range(1, nv):
        dest_start = ((q + k) % nv) * quarter
        send = lax.dynamic_slice_in_dim(amplitudes, dest_start, quarter, 2)
        pieces.append(lax.ppermute(send, "vb", [(i, (i + k) % nv) for i in range(nv)]))

    reversed_cols = jnp.concatenate(
        [integrals[:, ((-k) % nv) * quarter:((-k) % nv + 1) * quarter] for k in range(nv)], axis=1
    )
    rotated = roll_lanes(reversed_cols, qstart, 1)
    erows = -(-rows // width)
    erows_padded = -(-erows // 8) * 8
    energy_rows = jnp.pad(row_energy, (0, erows_padded * width - rows)).reshape(erows_padded, width)
    packed = jnp.concatenate([rotated, energy_rows], axis=0)

    remote = None
    scaled_blocks = []
    window = window_blocks(packed)
    for item in window:
        block = item[:rows]
        energies = item[rows:].reshape(-1)[:rows]
        weighted = None
        for k in range(nv):
            term = jnp.einsum(
                "rb,pba->rpa", block[:, k * quarter:(k + 1) * quarter], pieces[k], precision=PREC,
                preferred_element_type=jnp.float32,
            )
            weighted = term if weighted is None else weighted + term
        denom = (energies[:, None] + own_virtual[None, :])[:, None, :] - pair_energy[None, :, None]
        scaled = weighted / denom
        scaled_blocks.append((block, scaled))
        part = jnp.einsum(
            "rc,rpa->pca", block[:, quarter:], scaled, precision=PREC, preferred_element_type=jnp.float32
        )
        remote = part if remote is None else remote + part
    remote = with_layout_constraint(remote, Layout(major_to_minor=(0, 1, 2)))

    received = [None] * nv
    for k in range(1, nv):
        chunk = remote[:, (k - 1) * quarter:k * quarter]
        received[k] = lax.ppermute(chunk, "vb", [(i, (i - k) % nv) for i in range(nv)])
    own = None
    for block, scaled in scaled_blocks:
        part = jnp.einsum(
            "rc,rpa->pca", block[:, :quarter], scaled, precision=PREC, preferred_element_type=jnp.float32
        )
        own = part if own is None else own + part
    received[0] = with_layout_constraint(own, Layout(major_to_minor=(0, 1, 2)))
    out = jnp.zeros(received[0].shape[:2] + (width,), received[0].dtype)
    for k in range(nv):
        out = lax.dynamic_update_slice_in_dim(out, received[k], ((q + k) % nv) * quarter, 2)
    return out


def solution(mesh):
    return jax.shard_map(
        local,
        mesh=mesh,
        in_specs=(P("blk", "vb", None), P("blk", None), P("blk"), P("blk", None), P(), P()),
        out_specs=P("blk", "vb", None),
        check_vma=False,
    )
```
